256 devices in a mesh: chan: 64 (over y, z, core), ctr: 4 (over x).
Axes of the slice: x: 4, y: 4, z: 8, core: 2. Of those that a mesh axis runs over, the one named last changes fastest.
Arguments:
- amplitudes: float32 [4608, 64, 256], P('ctr', 'chan'), may hold values from -6 to 6
- pair_interaction: bfloat16 [64, 4608, 4608], P('chan', None, 'ctr'), may hold values from -0.09375 to 0.09375
- ph_interaction: float32 [128, 128, 128], P('chan'), may hold values from -0.5 to 0.5
- pp_size: int32 [64], P('chan'), may hold values from 1 to 72, as said below
- ph_owner: int32 [72, 64, 2], P('ctr', 'chan'), may hold values from 0 to 127, as said below
Outputs:
- residual: float32 [4608, 64, 256], P('ctr', 'chan')
The draws below stay inside these ranges and needn't reach their ends.
Inputs may be any that keep to these rules, and one draw needn't show every extreme that they name: Channel c has its first 64 * pp_size[c] particle pairs live; every draw has a channel with 72 live tiles. `ph_owner`: the ph channel g is owned by index g // 2 of chan. Of the 36 tiles that one device holds, at most 2 have ph channels owned by one index of chan; in every draw some index of chan receives exactly 2 tiles from every device.
All inputs are finite; a program needn't handle non-finite values.
Results may differ from the reference program's by a relative error of at most 0.002.
Values may be sent and summed in bfloat16 or wider, within the bound.
No kernel may reach another device: no remote copies, remote signals or barrier semaphores. Data moves between devices by JAX's collectives and lax.ppermute only.
A program may use at most 128 MiB of HBM per device.

```python
import jax
import jax.numpy as jnp
from jax import lax

TS = 64
TC = 128
K = 4608
HP = 256
PH_DEV = 2
CH_DEV = 1
CHANNELS = 64
PH = 128
RT = 72
TILES_DEV = 36
CAP = 2
N_CHAN = 64
N_CTR = 4


def draw_pp_size(key, part):
    counts = jax.random.randint(jax.random.fold_in(key, 11), (CHANNELS,), 1, RT + 1)
    picked = jax.random.randint(jax.random.fold_in(key, 12), (2,), 0, CHANNELS)
    places = jnp.arange(CHANNELS)
    counts = jnp.where(places == picked[0], RT, counts)
    counts = jnp.where((places == picked[1]) & (picked[1] != picked[0]), 1, counts)
    return counts.astype(jnp.int32)


def draw_ph_owner(key, part):
    slot_total = N_CHAN * CAP
    owner_zero = jax.random.randint(jax.random.fold_in(key, 21), (), 0, N_CHAN)

    def per_device(device_key):
        slot_order = jax.random.permutation(jax.random.fold_in(device_key, 1), slot_total)
        target = slot_order // CAP
        scores = jnp.where(target == owner_zero, 0, slot_total) + jnp.arange(slot_total)
        ranked = slot_order[jnp.argsort(scores)]
        chosen = ranked[:TILES_DEV]
        chosen = chosen[jax.random.permutation(jax.random.fold_in(device_key, 2), TILES_DEV)]
        within = jax.random.randint(jax.random.fold_in(device_key, 3), (TILES_DEV,), 0, PH_DEV)
        return chosen // CAP * PH_DEV + within
    device_keys = jax.random.split(jax.random.fold_in(key, 22), N_CTR * N_CHAN)
    values_all = jax.vmap(per_device)(device_keys)
    values_all = values_all.reshape(N_CTR, N_CHAN, RT // N_CTR, CH_DEV, HP // TC)
    values_all = jnp.transpose(values_all, (0, 2, 1, 3, 4)).reshape(RT, CHANNELS, HP // TC)
    return values_all.astype(jnp.int32)


def block_scale(stream_key, dims, shards, low, largest):
    def one(axis_at, parts):
        heights = jax.random.uniform(jax.random.fold_in(jax.random.fold_in(stream_key, 6), axis_at), (parts,), jnp.float32, low / len(shards), largest / len(shards))
        return jnp.repeat(jnp.exp(heights), dims[axis_at] // parts).reshape((-1,) + (1,) * (len(dims) - axis_at - 1))

    factor_of = one(*shards[0])
    for cut in shards[1:]:
        factor_of = factor_of * one(*cut)
    return factor_of


def gaussian(stream_key, dims, deviation, limit, cuts=(), held_as=jnp.bfloat16):
    result = deviation * jax.random.normal(stream_key, dims, jnp.float32)
    if cuts:
        result = result * block_scale(stream_key, dims, cuts, -0.22, 0.18)
    return jnp.clip(result, -limit, limit).astype(held_as)


def setup_inputs(seed: int = 0) -> dict:
    key_list = jax.random.split(jax.random.key(seed), 6)
    amplitudes = gaussian(key_list[0], (K, CHANNELS, HP), 1.0, 6.0, ((0, 4), (1, 64)), jnp.float32)
    pair_interaction = gaussian(key_list[1], (CHANNELS, K, K), K ** -0.5, 0.09375, ((0, 64), (2, 4)))
    ph_interaction = gaussian(key_list[2], (PH, TC, TC), TC ** -0.5, 0.5, ((0, 64),), jnp.float32)
    pp_size = draw_pp_size(jax.random.fold_in(key_list[5], 71), 0)
    ph_owner = draw_ph_owner(jax.random.fold_in(key_list[5], 71), 0)
    return dict(amplitudes=amplitudes, pair_interaction=pair_interaction, ph_interaction=ph_interaction, pp_size=pp_size, ph_owner=ph_owner)


def reference(amplitudes, pair_interaction, ph_interaction, pp_size, ph_owner):
    positions = jnp.arange(K, dtype=jnp.int32)
    live_mask = positions[:, None] < (pp_size * TS)[None, :]
    masked = jnp.where(live_mask[:, :, None], amplitudes, jnp.zeros_like(amplitudes))
    lowered = masked.astype(jnp.bfloat16)

    def ladder_one(channel):
        return jnp.dot(pair_interaction[channel], lowered[:, channel, :], preferred_element_type=jnp.float32)

    ladder = lax.map(ladder_one, jnp.arange(CHANNELS, dtype=jnp.int32))
    ladder = jnp.transpose(ladder, (1, 0, 2))
    blocks = masked.reshape(RT, TS, CHANNELS, HP // TC, TC)

    def cycle_one(index):
        chosen = ph_interaction[ph_owner[index]]
        return jnp.einsum("schk,chkl->schl", blocks[index], chosen, precision=lax.Precision.HIGHEST)

    cycle = lax.map(cycle_one, jnp.arange(RT, dtype=jnp.int32)).reshape(K, CHANNELS, HP)
    return jnp.where(live_mask[:, :, None], ladder, jnp.zeros_like(ladder)) + cycle
```

```python
import jax
import jax.numpy as jnp
from jax import lax
from jax.sharding import PartitionSpec as P


def local(amplitudes, pair_interaction, ph_interaction, pp_size, ph_owner):
    row_count, chan_count, hole_width = amplitudes.shape
    row_tiles, _, col_tiles = ph_owner.shape
    tile_rows = row_count // row_tiles
    tile_cols = hole_width // col_tiles
    ph_all = lax.all_gather(ph_interaction, "chan", axis=0, tiled=True)
    offset = lax.axis_index("ctr") * row_count
    positions = offset + jnp.arange(row_count, dtype=jnp.int32)
    live_mask = positions[:, None] < (pp_size * tile_rows)[None, :]
    masked = jnp.where(live_mask[:, :, None], amplitudes, jnp.zeros_like(amplitudes))
    lowered = masked.astype(jnp.bfloat16)
    ladder = lax.psum_scatter(
        jnp.einsum("crk,kch->rch", pair_interaction, lowered, preferred_element_type=jnp.float32),
        "ctr",
        scatter_dimension=0,
        tiled=True,
    )
    blocks = masked.reshape(row_tiles, tile_rows, chan_count, col_tiles, tile_cols)
    chosen = ph_all[ph_owner]
    cycle = jnp.einsum(
        "rschk,rchkl->rschl", blocks, chosen, precision=lax.Precision.HIGHEST
    ).reshape(row_count, chan_count, hole_width)
    return jnp.where(live_mask[:, :, None], ladder, jnp.zeros_like(ladder)) + cycle


def solution(mesh):
    in_specs = (
        P("ctr", "chan", None),
        P("chan", None, "ctr"),
        P("chan", None, None),
        P("chan"),
        P("ctr", "chan", None),
    )
    out_specs = P("ctr", "chan", None)
    return jax.shard_map(local, mesh=mesh, in_specs=in_specs, out_specs=out_specs, check_vma=False)
```

```python
import jax
import jax.numpy as jnp
from jax import lax
from jax.sharding import Mesh
from jax.sharding import PartitionSpec as P

CHAN = ("cy", "cz", "core")


def local(amplitudes, pair_interaction, ph_interaction, pp_size, ph_owner):
    row_count, chan_count, hole_width = amplitudes.shape
    row_tiles, _, col_tiles = ph_owner.shape
    tile_rows = row_count // row_tiles
    tile_cols = hole_width // col_tiles
    per_dev = ph_interaction.shape[0]
    cores = lax.axis_size("core")
    half = lax.all_gather(ph_interaction, ("cy", "cz"), axis=0, tiled=False)
    ph_all = lax.all_gather(half, "core", axis=1, tiled=False)
    ph_all = ph_all.reshape((-1,) + ph_interaction.shape[1:])
    offset = lax.axis_index("ctr") * row_count
    positions = offset + jnp.arange(row_count, dtype=jnp.int32)
    live_mask = positions[:, None] < (pp_size * tile_rows)[None, :]
    masked = jnp.where(live_mask[:, :, None], amplitudes, jnp.zeros_like(amplitudes))
    lowered = masked.astype(jnp.bfloat16)
    ladder = lax.psum_scatter(
        jnp.einsum("crk,kch->rch", pair_interaction, lowered, preferred_element_type=jnp.float32),
        "ctr",
        scatter_dimension=0,
        tiled=True,
    )
    blocks = masked.reshape(row_tiles, tile_rows, chan_count, col_tiles, tile_cols)
    chosen = ph_all[ph_owner]
    cycle = jnp.einsum(
        "rschk,rchkl->rschl", blocks, chosen, precision=lax.Precision.HIGHEST
    ).reshape(row_count, chan_count, hole_width)
    return jnp.where(live_mask[:, :, None], ladder, jnp.zeros_like(ladder)) + cycle


def solution(mesh):
    chan_size, ctr_size = mesh.devices.shape
    cores = 2
    cz = 8
    fine = Mesh(
        mesh.devices.reshape(chan_size // (cz * cores), cz, cores, ctr_size),
        CHAN + ("ctr",),
    )
    in_specs = (
        P("ctr", CHAN, None),
        P(CHAN, None, "ctr"),
        P(CHAN, None, None),
        P(CHAN),
        P("ctr", CHAN, None),
    )
    out_specs = P("ctr", CHAN, None)
    return jax.shard_map(local, mesh=fine, in_specs=in_specs, out_specs=out_specs, check_vma=False)
```

```python
import jax
import jax.numpy as jnp
from jax import lax
from jax.sharding import Mesh
from jax.sharding import PartitionSpec as P

CHAN = ("cy", "cz", "core")


def shift(x, axis, step):
    n = lax.axis_size(axis)
    return lax.ppermute(x, axis, [(k, (k + step) % n) for k in range(n)])


def ring_gather(x, axis):
    n = lax.axis_size(axis)
    up = [x]
    down = [x]
    for _ in range((n - 1) // 2):
        up.append(shift(up[-1], axis, -1))
        down.append(shift(down[-1], axis, 1))
    pieces = up
    if n % 2 == 0:
        cut = x.shape[0] // 2
        far = jnp.concatenate(
            [shift(up[-1][:cut], axis, -1), shift(down[-1][cut:], axis, 1)], axis=0
        )
        pieces = pieces + [far]
    pieces = pieces + down[1:][::-1]
    return jnp.stack(pieces, axis=0)


def local(amplitudes, pair_interaction, ph_interaction, pp_size, ph_owner):
    row_count, chan_count, hole_width = amplitudes.shape
    row_tiles, _, col_tiles = ph_owner.shape
    tile_rows = row_count // row_tiles
    tile_cols = hole_width // col_tiles
    per_dev = ph_interaction.shape[0]
    ny, nz, nc = lax.axis_size("cy"), lax.axis_size("cz"), lax.axis_size("core")
    gathered = ring_gather(ph_interaction, "cz")
    gathered = ring_gather(gathered, "cy")
    gathered = jnp.stack([gathered, shift(gathered, "core", 1)], axis=0)
    ph_all = gathered.reshape((-1,) + ph_interaction.shape[1:])
    offset = lax.axis_index("ctr") * row_count
    positions = offset + jnp.arange(row_count, dtype=jnp.int32)
    live_mask = positions[:, None] < (pp_size * tile_rows)[None, :]
    masked = jnp.where(live_mask[:, :, None], amplitudes, jnp.zeros_like(amplitudes))
    lowered = masked.astype(jnp.bfloat16)
    ladder = lax.psum_scatter(
        jnp.einsum("crk,kch->rch", pair_interaction, lowered, preferred_element_type=jnp.float32),
        "ctr",
        scatter_dimension=0,
        tiled=True,
    )
    owner_dev = ph_owner // per_dev
    o_y = (owner_dev // (nz * nc) - lax.axis_index("cy")) % ny
    o_z = (owner_dev // nc % nz - lax.axis_index("cz")) % nz
    o_c = (owner_dev % nc - lax.axis_index("core")) % nc
    slot = ((o_c * ny + o_y) * nz + o_z) * per_dev + ph_owner % per_dev
    blocks = masked.reshape(row_tiles, tile_rows, chan_count, col_tiles, tile_cols)
    chosen = ph_all[slot]
    cycle = jnp.einsum(
        "rschk,rchkl->rschl", blocks, chosen, precision=lax.Precision.HIGHEST
    ).reshape(row_count, chan_count, hole_width)
    return jnp.where(live_mask[:, :, None], ladder, jnp.zeros_like(ladder)) + cycle


def solution(mesh):
    chan_size, ctr_size = mesh.devices.shape
    cores = 2
    cz = 8
    fine = Mesh(
        mesh.devices.reshape(chan_size // (cz * cores), cz, cores, ctr_size),
        CHAN + ("ctr",),
    )
    in_specs = (
        P("ctr", CHAN, None),
        P(CHAN, None, "ctr"),
        P(CHAN, None, None),
        P(CHAN),
        P("ctr", CHAN, None),
    )
    out_specs = P("ctr", CHAN, None)
    return jax.shard_map(local, mesh=fine, in_specs=in_specs, out_specs=out_specs, check_vma=False)
```

```python
import jax
import jax.numpy as jnp
from jax import lax
from jax.sharding import Mesh
from jax.sharding import PartitionSpec as P

CHAN = ("cy", "cz", "core")


def shift(x, axis, step):
    n = lax.axis_size(axis)
    return lax.ppermute(x, axis, [(k, (k + step) % n) for k in range(n)])


def ring_gather(x, axis):
    n = lax.axis_size(axis)
    up = [x]
    down = [x]
    for _ in range((n - 1) // 2):
        up.append(shift(up[-1], axis, -1))
        down.append(shift(down[-1], axis, 1))
    pieces = up
    if n % 2 == 0:
        cut = x.shape[0] // 2
        far = jnp.concatenate(
            [shift(up[-1][:cut], axis, -1), shift(down[-1][cut:], axis, 1)], axis=0
        )
        pieces = pieces + [far]
    pieces = pieces + down[1:][::-1]
    return jnp.stack(pieces, axis=0)


def local(amplitudes, pair_interaction, ph_interaction, pp_size, ph_owner):
    row_count, chan_count, hole_width = amplitudes.shape
    row_tiles, _, col_tiles = ph_owner.shape
    tile_rows = row_count // row_tiles
    tile_cols = hole_width // col_tiles
    per_dev = ph_interaction.shape[0]
    ny, nz, nc = lax.axis_size("cy"), lax.axis_size("cz"), lax.axis_size("core")
    by_z = ring_gather(ph_interaction, "cz")
    own = lax.all_gather(by_z, "cy", axis=0, tiled=False)
    own = own.reshape((-1,) + ph_interaction.shape[1:])
    sibling = shift(own, "core", 1)
    offset = lax.axis_index("ctr") * row_count
    positions = offset + jnp.arange(row_count, dtype=jnp.int32)
    live_mask = positions[:, None] < (pp_size * tile_rows)[None, :]
    masked = jnp.where(live_mask[:, :, None], amplitudes, jnp.zeros_like(amplitudes))
    lowered = masked.astype(jnp.bfloat16)
    ladder = lax.psum_scatter(
        jnp.einsum("crk,kch->rch", pair_interaction, lowered, preferred_element_type=jnp.float32),
        "ctr",
        scatter_dimension=0,
        tiled=True,
    )
    owner_dev = ph_owner // per_dev
    o_y = owner_dev // (nz * nc)
    o_z = (owner_dev // nc % nz - lax.axis_index("cz")) % nz
    o_c = (owner_dev % nc - lax.axis_index("core")) % nc
    slot = (o_y * nz + o_z) * per_dev + ph_owner % per_dev
    blocks = masked.reshape(row_tiles, tile_rows, chan_count, col_tiles, tile_cols)
    chosen = jnp.where((o_c == 0)[..., None, None], own[slot], sibling[slot])
    cycle = jnp.einsum(
        "rschk,rchkl->rschl", blocks, chosen, precision=lax.Precision.HIGHEST
    ).reshape(row_count, chan_count, hole_width)
    return jnp.where(live_mask[:, :, None], ladder, jnp.zeros_like(ladder)) + cycle


def solution(mesh):
    chan_size, ctr_size = mesh.devices.shape
    cores = 2
    cz = 8
    fine = Mesh(
        mesh.devices.reshape(chan_size // (cz * cores), cz, cores, ctr_size),
        CHAN + ("ctr",),
    )
    in_specs = (
        P("ctr", CHAN, None),
        P(CHAN, None, "ctr"),
        P(CHAN, None, None),
        P(CHAN),
        P("ctr", CHAN, None),
    )
    out_specs = P("ctr", CHAN, None)
    return jax.shard_map(local, mesh=fine, in_specs=in_specs, out_specs=out_specs, check_vma=False)
```

```python
import jax
import jax.numpy as jnp
from jax import lax
from jax.sharding import Mesh
from jax.sharding import PartitionSpec as P

CHAN = ("cy", "cz", "core")


def shift(x, axis, step):
    n = lax.axis_size(axis)
    return lax.ppermute(x, axis, [(k, (k + step) % n) for k in range(n)])


def ring_gather(x, axis):
    n = lax.axis_size(axis)
    up = [x]
    down = [x]
    for _ in range((n - 1) // 2):
        up.append(shift(up[-1], axis, -1))
        down.append(shift(down[-1], axis, 1))
    pieces = up
    if n % 2 == 0:
        cut = x.shape[0] // 2
        far = jnp.concatenate(
            [shift(up[-1][:cut], axis, -1), shift(down[-1][cut:], axis, 1)], axis=0
        )
        pieces = pieces + [far]
    pieces = pieces + down[1:][::-1]
    return jnp.stack(pieces, axis=0)


def direct_gather(x, axis):
    n = lax.axis_size(axis)
    return jnp.stack([x] + [shift(x, axis, -o) for o in range(1, n)], axis=0)


def local(amplitudes, pair_interaction, ph_interaction, pp_size, ph_owner):
    row_count, chan_count, hole_width = amplitudes.shape
    row_tiles, _, col_tiles = ph_owner.shape
    tile_rows = row_count // row_tiles
    tile_cols = hole_width // col_tiles
    per_dev = ph_interaction.shape[0]
    ny, nz, nc = lax.axis_size("cy"), lax.axis_size("cz"), lax.axis_size("core")
    by_z = direct_gather(ph_interaction, "cz")
    own = lax.all_gather(by_z, "cy", axis=0, tiled=False)
    own = own.reshape((-1,) + ph_interaction.shape[1:])
    sibling = shift(own, "core", 1)
    offset = lax.axis_index("ctr") * row_count
    positions = offset + jnp.arange(row_count, dtype=jnp.int32)
    live_mask = positions[:, None] < (pp_size * tile_rows)[None, :]
    masked = jnp.where(live_mask[:, :, None], amplitudes, jnp.zeros_like(amplitudes))
    lowered = masked.astype(jnp.bfloat16)
    ladder = lax.psum_scatter(
        jnp.einsum("crk,kch->rch", pair_interaction, lowered, preferred_element_type=jnp.float32),
        "ctr",
        scatter_dimension=0,
        tiled=True,
    )
    owner_dev = ph_owner // per_dev
    o_y = owner_dev // (nz * nc)
    o_z = (owner_dev // nc % nz - lax.axis_index("cz")) % nz
    o_c = (owner_dev % nc - lax.axis_index("core")) % nc
    slot = (o_y * nz + o_z) * per_dev + ph_owner % per_dev
    blocks = masked.reshape(row_tiles, tile_rows, chan_count, col_tiles, tile_cols)
    chosen = jnp.where((o_c == 0)[..., None, None], own[slot], sibling[slot])
    cycle = jnp.einsum(
        "rschk,rchkl->rschl", blocks, chosen, precision=lax.Precision.HIGHEST
    ).reshape(row_count, chan_count, hole_width)
    return jnp.where(live_mask[:, :, None], ladder, jnp.zeros_like(ladder)) + cycle


def solution(mesh):
    chan_size, ctr_size = mesh.devices.shape
    cores = 2
    cz = 8
    fine = Mesh(
        mesh.devices.reshape(chan_size // (cz * cores), cz, cores, ctr_size),
        CHAN + ("ctr",),
    )
    in_specs = (
        P("ctr", CHAN, None),
        P(CHAN, None, "ctr"),
        P(CHAN, None, None),
        P(CHAN),
        P("ctr", CHAN, None),
    )
    out_specs = P("ctr", CHAN, None)
    return jax.shard_map(local, mesh=fine, in_specs=in_specs, out_specs=out_specs, check_vma=False)
```

```python
import jax
import jax.numpy as jnp
from jax import lax
from jax.sharding import PartitionSpec as P


def local(amplitudes, pair_interaction, ph_interaction, pp_size, ph_owner):
    row_count, chan_count, hole_width = amplitudes.shape
    row_tiles, _, col_tiles = ph_owner.shape
    tile_rows = row_count // row_tiles
    tile_cols = hole_width // col_tiles
    ph_all = lax.all_gather(ph_interaction, "chan", axis=0, tiled=True)
    offset = lax.axis_index("ctr") * row_count
    positions = offset + jnp.arange(row_count, dtype=jnp.int32)
    live = (positions < pp_size[0] * tile_rows)[:, None]
    flat = amplitudes.reshape(row_count, hole_width)
    masked = jnp.where(live, flat, jnp.zeros_like(flat))
    lowered = masked.astype(jnp.bfloat16)
    ladder = lax.psum_scatter(
        jnp.dot(pair_interaction[0], lowered, preferred_element_type=jnp.float32),
        "ctr",
        scatter_dimension=0,
        tiled=True,
    )
    blocks = masked.reshape(row_tiles, tile_rows, col_tiles, tile_cols)
    chosen = ph_all[ph_owner[:, 0, :]]
    ladder = jnp.where(live, ladder, jnp.zeros_like(ladder))
    ladder = ladder.reshape(row_tiles, tile_rows, col_tiles, tile_cols)
    residual = ladder + jnp.einsum(
        "rshk,rhkl->rshl", blocks, chosen, precision=lax.Precision.HIGHEST
    )
    return residual.reshape(row_count, chan_count, hole_width)


def solution(mesh):
    in_specs = (
        P("ctr", "chan", None),
        P("chan", None, "ctr"),
        P("chan", None, None),
        P("chan"),
        P("ctr", "chan", None),
    )
    out_specs = P("ctr", "chan", None)
    return jax.shard_map(local, mesh=mesh, in_specs=in_specs, out_specs=out_specs, check_vma=False)
```

```python
import jax
import jax.numpy as jnp
from jax import lax
from jax.sharding import Mesh
from jax.sharding import PartitionSpec as P

CHAN = ("cy", "cz", "core")


def shift(x, axis, step):
    n = lax.axis_size(axis)
    return lax.ppermute(x, axis, [(k, (k + step) % n) for k in range(n)])


def ring_gather(x, axis):
    n = lax.axis_size(axis)
    up = [x]
    down = [x]
    for _ in range((n - 1) // 2):
        up.append(shift(up[-1], axis, -1))
        down.append(shift(down[-1], axis, 1))
    pieces = up
    if n % 2 == 0:
        cut = x.shape[0] // 2
        far = jnp.concatenate(
            [shift(up[-1][:cut], axis, -1), shift(down[-1][cut:], axis, 1)], axis=0
        )
        pieces = pieces + [far]
    pieces = pieces + down[1:][::-1]
    return jnp.stack(pieces, axis=0)


def direct_gather(x, axis):
    n = lax.axis_size(axis)
    return jnp.stack([x] + [shift(x, axis, -o) for o in range(1, n)], axis=0)


def local(amplitudes, pair_interaction, ph_interaction, pp_size, ph_owner):
    row_count, chan_count, hole_width = amplitudes.shape
    row_tiles, _, col_tiles = ph_owner.shape
    tile_rows = row_count // row_tiles
    tile_cols = hole_width // col_tiles
    per_dev = ph_interaction.shape[0]
    ny, nz, nc = lax.axis_size("cy"), lax.axis_size("cz"), lax.axis_size("core")
    by_y = lax.all_gather(ph_interaction, "cy", axis=0, tiled=False)
    own = lax.all_gather(by_y, "cz", axis=0, tiled=False)
    own = own.reshape((-1,) + ph_interaction.shape[1:])
    sibling = shift(own, "core", 1)
    offset = lax.axis_index("ctr") * row_count
    positions = offset + jnp.arange(row_count, dtype=jnp.int32)
    live_mask = positions[:, None] < (pp_size * tile_rows)[None, :]
    masked = jnp.where(live_mask[:, :, None], amplitudes, jnp.zeros_like(amplitudes))
    lowered = masked.astype(jnp.bfloat16)
    ladder = lax.psum_scatter(
        jnp.einsum("crk,kch->rch", pair_interaction, lowered, preferred_element_type=jnp.float32),
        "ctr",
        scatter_dimension=0,
        tiled=True,
    )
    owner_dev = ph_owner // per_dev
    o_y = owner_dev // (nz * nc)
    o_z = owner_dev // nc % nz
    o_c = (owner_dev % nc - lax.axis_index("core")) % nc
    slot = (o_z * ny + o_y) * per_dev + ph_owner % per_dev
    blocks = masked.reshape(row_tiles, tile_rows, chan_count, col_tiles, tile_cols)
    chosen = jnp.where((o_c == 0)[..., None, None], own[slot], sibling[slot])
    cycle = jnp.einsum(
        "rschk,rchkl->rschl", blocks, chosen, precision=lax.Precision.HIGHEST
    ).reshape(row_count, chan_count, hole_width)
    return jnp.where(live_mask[:, :, None], ladder, jnp.zeros_like(ladder)) + cycle


def solution(mesh):
    chan_size, ctr_size = mesh.devices.shape
    cores = 2
    cz = 8
    fine = Mesh(
        mesh.devices.reshape(chan_size // (cz * cores), cz, cores, ctr_size),
        CHAN + ("ctr",),
    )
    in_specs = (
        P("ctr", CHAN, None),
        P(CHAN, None, "ctr"),
        P(CHAN, None, None),
        P(CHAN),
        P("ctr", CHAN, None),
    )
    out_specs = P("ctr", CHAN, None)
    return jax.shard_map(local, mesh=fine, in_specs=in_specs, out_specs=out_specs, check_vma=False)
```

```python
import jax
import jax.numpy as jnp
from jax import lax
from jax.sharding import Mesh
from jax.sharding import PartitionSpec as P

CHAN = ("cy", "cz", "core")


def shift(x, axis, step):
    n = lax.axis_size(axis)
    return lax.ppermute(x, axis, [(k, (k + step) % n) for k in range(n)])


def ring_gather(x, axis):
    n = lax.axis_size(axis)
    up = [x]
    down = [x]
    for _ in range((n - 1) // 2):
        up.append(shift(up[-1], axis, -1))
        down.append(shift(down[-1], axis, 1))
    pieces = up
    if n % 2 == 0:
        cut = x.shape[0] // 2
        far = jnp.concatenate(
            [shift(up[-1][:cut], axis, -1), shift(down[-1][cut:], axis, 1)], axis=0
        )
        pieces = pieces + [far]
    pieces = pieces + down[1:][::-1]
    return jnp.stack(pieces, axis=0)


def direct_gather(x, axis):
    n = lax.axis_size(axis)
    return jnp.stack([x] + [shift(x, axis, -o) for o in range(1, n)], axis=0)


def local(amplitudes, pair_interaction, ph_interaction, pp_size, ph_owner):
    row_count, chan_count, hole_width = amplitudes.shape
    row_tiles, _, col_tiles = ph_owner.shape
    tile_rows = row_count // row_tiles
    tile_cols = hole_width // col_tiles
    per_dev = ph_interaction.shape[0]
    ny, nz, nc = lax.axis_size("cy"), lax.axis_size("cz"), lax.axis_size("core")
    by_y = lax.all_gather(ph_interaction, ("cy", "ctr"), axis=0, tiled=False).reshape((-1, 4) + ph_interaction.shape)[:, 0]
    own = lax.all_gather(by_y, "cz", axis=0, tiled=False)
    own = own.reshape((-1,) + ph_interaction.shape[1:])
    sibling = shift(own, "core", 1)
    offset = lax.axis_index("ctr") * row_count
    positions = offset + jnp.arange(row_count, dtype=jnp.int32)
    live_mask = positions[:, None] < (pp_size * tile_rows)[None, :]
    masked = jnp.where(live_mask[:, :, None], amplitudes, jnp.zeros_like(amplitudes))
    lowered = masked.astype(jnp.bfloat16)
    ladder = lax.psum_scatter(
        jnp.einsum("crk,kch->rch", pair_interaction, lowered, preferred_element_type=jnp.float32),
        "ctr",
        scatter_dimension=0,
        tiled=True,
    )
    owner_dev = ph_owner // per_dev
    o_y = owner_dev // (nz * nc)
    o_z = owner_dev // nc % nz
    o_c = (owner_dev % nc - lax.axis_index("core")) % nc
    slot = (o_z * ny + o_y) * per_dev + ph_owner % per_dev
    blocks = masked.reshape(row_tiles, tile_rows, chan_count, col_tiles, tile_cols)
    chosen = jnp.where((o_c == 0)[..., None, None], own[slot], sibling[slot])
    cycle = jnp.einsum(
        "rschk,rchkl->rschl", blocks, chosen, precision=lax.Precision.HIGHEST
    ).reshape(row_count, chan_count, hole_width)
    return jnp.where(live_mask[:, :, None], ladder, jnp.zeros_like(ladder)) + cycle


def solution(mesh):
    chan_size, ctr_size = mesh.devices.shape
    cores = 2
    cz = 8
    fine = Mesh(
        mesh.devices.reshape(chan_size // (cz * cores), cz, cores, ctr_size),
        CHAN + ("ctr",),
    )
    in_specs = (
        P("ctr", CHAN, None),
        P(CHAN, None, "ctr"),
        P(CHAN, None, None),
        P(CHAN),
        P("ctr", CHAN, None),
    )
    out_specs = P("ctr", CHAN, None)
    return jax.shard_map(local, mesh=fine, in_specs=in_specs, out_specs=out_specs, check_vma=False)
```

```python
import jax
import jax.numpy as jnp
from jax import lax
from jax.experimental import pallas as pl
from jax.sharding import Mesh
from jax.sharding import PartitionSpec as P

CHAN = ("cy", "cz", "core")


def shift(x, axis, step):
    n = lax.axis_size(axis)
    return lax.ppermute(x, axis, [(k, (k + step) % n) for k in range(n)])


def ring_gather(x, axis):
    n = lax.axis_size(axis)
    up = [x]
    down = [x]
    for _ in range((n - 1) // 2):
        up.append(shift(up[-1], axis, -1))
        down.append(shift(down[-1], axis, 1))
    pieces = up
    if n % 2 == 0:
        cut = x.shape[0] // 2
        far = jnp.concatenate(
            [shift(up[-1][:cut], axis, -1), shift(down[-1][cut:], axis, 1)], axis=0
        )
        pieces = pieces + [far]
    pieces = pieces + down[1:][::-1]
    return jnp.stack(pieces, axis=0)


def direct_gather(x, axis):
    n = lax.axis_size(axis)
    return jnp.stack([x] + [shift(x, axis, -o) for o in range(1, n)], axis=0)


def ladder_kernel(p_ref, l_ref, o_ref):
    o_ref[...] = jnp.dot(p_ref[...], l_ref[...], preferred_element_type=jnp.float32)


def ladder_matmul(weights, lowered, block=512):
    rows, depth = weights.shape
    width = lowered.shape[1]
    return pl.pallas_call(
        ladder_kernel,
        grid=(rows // block,),
        in_specs=[
            pl.BlockSpec((block, depth), lambda i: (i, 0)),
            pl.BlockSpec((depth, width), lambda i: (0, 0)),
        ],
        out_specs=pl.BlockSpec((block, width), lambda i: (i, 0)),
        out_shape=jax.ShapeDtypeStruct((rows, width), jnp.float32),
        cost_estimate=pl.CostEstimate(
            flops=2 * rows * depth * width,
            bytes_accessed=2 * rows * depth + 2 * depth * width + 4 * rows * width,
            transcendentals=0,
        ),
    )(weights, lowered)


def local(amplitudes, pair_interaction, ph_interaction, pp_size, ph_owner):
    row_count, chan_count, hole_width = amplitudes.shape
    row_tiles, _, col_tiles = ph_owner.shape
    tile_rows = row_count // row_tiles
    tile_cols = hole_width // col_tiles
    per_dev = ph_interaction.shape[0]
    ny, nz, nc = lax.axis_size("cy"), lax.axis_size("cz"), lax.axis_size("core")
    by_y = lax.all_gather(ph_interaction, "cy", axis=0, tiled=False)
    own = lax.all_gather(by_y, "cz", axis=0, tiled=False)
    own = own.reshape((-1,) + ph_interaction.shape[1:])
    sibling = shift(own, "core", 1)
    offset = lax.axis_index("ctr") * row_count
    positions = offset + jnp.arange(row_count, dtype=jnp.int32)
    live_mask = positions[:, None] < (pp_size * tile_rows)[None, :]
    masked = jnp.where(live_mask[:, :, None], amplitudes, jnp.zeros_like(amplitudes))
    lowered = masked.reshape(row_count, hole_width).astype(jnp.bfloat16)
    ladder = lax.psum_scatter(
        ladder_matmul(pair_interaction[0], lowered),
        "ctr",
        scatter_dimension=0,
        tiled=True,
    ).reshape(row_count, chan_count, hole_width)
    owner_dev = ph_owner // per_dev
    o_y = owner_dev // (nz * nc)
    o_z = owner_dev // nc % nz
    o_c = (owner_dev % nc - lax.axis_index("core")) % nc
    slot = (o_z * ny + o_y) * per_dev + ph_owner % per_dev
    blocks = masked.reshape(row_tiles, tile_rows, chan_count, col_tiles, tile_cols)
    chosen = jnp.where((o_c == 0)[..., None, None], own[slot], sibling[slot])
    cycle = jnp.einsum(
        "rschk,rchkl->rschl", blocks, chosen, precision=lax.Precision.HIGHEST
    ).reshape(row_count, chan_count, hole_width)
    return jnp.where(live_mask[:, :, None], ladder, jnp.zeros_like(ladder)) + cycle


def solution(mesh):
    chan_size, ctr_size = mesh.devices.shape
    cores = 2
    cz = 8
    fine = Mesh(
        mesh.devices.reshape(chan_size // (cz * cores), cz, cores, ctr_size),
        CHAN + ("ctr",),
    )
    in_specs = (
        P("ctr", CHAN, None),
        P(CHAN, None, "ctr"),
        P(CHAN, None, None),
        P(CHAN),
        P("ctr", CHAN, None),
    )
    out_specs = P("ctr", CHAN, None)
    return jax.shard_map(local, mesh=fine, in_specs=in_specs, out_specs=out_specs, check_vma=False)
```

```python
import jax
import jax.numpy as jnp
from jax import lax
from jax.sharding import Mesh
from jax.sharding import PartitionSpec as P

CHAN = ("cy", "cz", "core")


def shift(x, axis, step):
    n = lax.axis_size(axis)
    return lax.ppermute(x, axis, [(k, (k + step) % n) for k in range(n)])


def ring_gather(x, axis):
    n = lax.axis_size(axis)
    up = [x]
    down = [x]
    for _ in range((n - 1) // 2):
        up.append(shift(up[-1], axis, -1))
        down.append(shift(down[-1], axis, 1))
    pieces = up
    if n % 2 == 0:
        cut = x.shape[0] // 2
        far = jnp.concatenate(
            [shift(up[-1][:cut], axis, -1), shift(down[-1][cut:], axis, 1)], axis=0
        )
        pieces = pieces + [far]
    pieces = pieces + down[1:][::-1]
    return jnp.stack(pieces, axis=0)


def direct_gather(x, axis):
    n = lax.axis_size(axis)
    return jnp.stack([x] + [shift(x, axis, -o) for o in range(1, n)], axis=0)


def local(amplitudes, pair_interaction, ph_interaction, pp_size, ph_owner):
    row_count, chan_count, hole_width = amplitudes.shape
    row_tiles, _, col_tiles = ph_owner.shape
    tile_rows = row_count // row_tiles
    tile_cols = hole_width // col_tiles
    per_dev = ph_interaction.shape[0]
    ny, nz, nc = lax.axis_size("cy"), lax.axis_size("cz"), lax.axis_size("core")
    by_y = ring_gather(ph_interaction, "cy")
    own = lax.all_gather(by_y, "cz", axis=0, tiled=False)
    own = own.reshape((-1,) + ph_interaction.shape[1:])
    sibling = shift(own, "core", 1)
    offset = lax.axis_index("ctr") * row_count
    positions = offset + jnp.arange(row_count, dtype=jnp.int32)
    live_mask = positions[:, None] < (pp_size * tile_rows)[None, :]
    masked = jnp.where(live_mask[:, :, None], amplitudes, jnp.zeros_like(amplitudes))
    lowered = masked.astype(jnp.bfloat16)
    ladder = lax.psum_scatter(
        jnp.einsum("crk,kch->rch", pair_interaction, lowered, preferred_element_type=jnp.float32),
        "ctr",
        scatter_dimension=0,
        tiled=True,
    )
    owner_dev = ph_owner // per_dev
    o_y = (owner_dev // (nz * nc) - lax.axis_index("cy")) % ny
    o_z = owner_dev // nc % nz
    o_c = (owner_dev % nc - lax.axis_index("core")) % nc
    slot = (o_z * ny + o_y) * per_dev + ph_owner % per_dev
    blocks = masked.reshape(row_tiles, tile_rows, chan_count, col_tiles, tile_cols)
    chosen = jnp.where((o_c == 0)[..., None, None], own[slot], sibling[slot])
    cycle = jnp.einsum(
        "rschk,rchkl->rschl", blocks, chosen, precision=lax.Precision.HIGHEST
    ).reshape(row_count, chan_count, hole_width)
    return jnp.where(live_mask[:, :, None], ladder, jnp.zeros_like(ladder)) + cycle


def solution(mesh):
    chan_size, ctr_size = mesh.devices.shape
    cores = 2
    cz = 8
    fine = Mesh(
        mesh.devices.reshape(chan_size // (cz * cores), cz, cores, ctr_size),
        CHAN + ("ctr",),
    )
    in_specs = (
        P("ctr", CHAN, None),
        P(CHAN, None, "ctr"),
        P(CHAN, None, None),
        P(CHAN),
        P("ctr", CHAN, None),
    )
    out_specs = P("ctr", CHAN, None)
    return jax.shard_map(local, mesh=fine, in_specs=in_specs, out_specs=out_specs, check_vma=False)
```

```python
import jax
import jax.numpy as jnp
from jax import lax
from jax.sharding import Mesh
from jax.sharding import PartitionSpec as P

CHAN = ("cy", "cz", "core")


def shift(x, axis, step):
    n = lax.axis_size(axis)
    return lax.ppermute(x, axis, [(k, (k + step) % n) for k in range(n)])


def ring_gather(x, axis):
    n = lax.axis_size(axis)
    up = [x]
    down = [x]
    for _ in range((n - 1) // 2):
        up.append(shift(up[-1], axis, -1))
        down.append(shift(down[-1], axis, 1))
    pieces = up
    if n % 2 == 0:
        cut = x.shape[0] // 2
        far = jnp.concatenate(
            [shift(up[-1][:cut], axis, -1), shift(down[-1][cut:], axis, 1)], axis=0
        )
        pieces = pieces + [far]
    pieces = pieces + down[1:][::-1]
    return jnp.stack(pieces, axis=0)


def direct_gather(x, axis):
    n = lax.axis_size(axis)
    return jnp.stack([x] + [shift(x, axis, -o) for o in range(1, n)], axis=0)


def local(amplitudes, pair_interaction, ph_interaction, pp_size, ph_owner):
    row_count, chan_count, hole_width = amplitudes.shape
    row_tiles, _, col_tiles = ph_owner.shape
    tile_rows = row_count // row_tiles
    tile_cols = hole_width // col_tiles
    per_dev = ph_interaction.shape[0]
    ny, nz, nc = lax.axis_size("cy"), lax.axis_size("cz"), lax.axis_size("core")
    by_y = lax.all_gather(ph_interaction, "cy", axis=0, tiled=False)
    own = lax.all_gather(by_y, "cz", axis=0, tiled=False)
    own = own.reshape((-1,) + ph_interaction.shape[1:])
    offset = lax.axis_index("ctr") * row_count
    positions = offset + jnp.arange(row_count, dtype=jnp.int32)
    live_mask = positions[:, None] < (pp_size * tile_rows)[None, :]
    masked = jnp.where(live_mask[:, :, None], amplitudes, jnp.zeros_like(amplitudes))
    lowered = masked.astype(jnp.bfloat16)
    my_core = lax.axis_index("core")

    def place(owner):
        dev = owner // per_dev
        here = ((dev // nc % nz) * ny + dev // (nz * nc)) * per_dev + owner % per_dev
        return here, dev % nc

    slot, owner_core = place(ph_owner)
    sib_slot, _ = place(shift(ph_owner, "core", 1))
    blocks = masked.reshape(row_tiles, tile_rows, chan_count, col_tiles, tile_cols)
    slot, sib_slot, blocks, lowered = lax.optimization_barrier((slot, sib_slot, blocks, lowered))
    ladder = lax.psum_scatter(
        jnp.einsum("crk,kch->rch", pair_interaction, lowered, preferred_element_type=jnp.float32),
        "ctr",
        scatter_dimension=0,
        tiled=True,
    )
    from_sibling = shift(own[sib_slot], "core", 1)
    chosen = jnp.where((owner_core == my_core)[..., None, None], own[slot], from_sibling)
    cycle = jnp.einsum(
        "rschk,rchkl->rschl", blocks, chosen, precision=lax.Precision.HIGHEST
    ).reshape(row_count, chan_count, hole_width)
    return jnp.where(live_mask[:, :, None], ladder, jnp.zeros_like(ladder)) + cycle


def solution(mesh):
    chan_size, ctr_size = mesh.devices.shape
    cores = 2
    cz = 8
    fine = Mesh(
        mesh.devices.reshape(chan_size // (cz * cores), cz, cores, ctr_size),
        CHAN + ("ctr",),
    )
    in_specs = (
        P("ctr", CHAN, None),
        P(CHAN, None, "ctr"),
        P(CHAN, None, None),
        P(CHAN),
        P("ctr", CHAN, None),
    )
    out_specs = P("ctr", CHAN, None)
    return jax.shard_map(local, mesh=fine, in_specs=in_specs, out_specs=out_specs, check_vma=False)
```

```python
import jax
import jax.numpy as jnp
from jax import lax
from jax.sharding import Mesh
from jax.sharding import PartitionSpec as P

CHAN = ("cy", "cz", "core")


def shift(x, axis, step):
    n = lax.axis_size(axis)
    return lax.ppermute(x, axis, [(k, (k + step) % n) for k in range(n)])


def ring_gather(x, axis):
    n = lax.axis_size(axis)
    up = [x]
    down = [x]
    for _ in range((n - 1) // 2):
        up.append(shift(up[-1], axis, -1))
        down.append(shift(down[-1], axis, 1))
    pieces = up
    if n % 2 == 0:
        cut = x.shape[0] // 2
        far = jnp.concatenate(
            [shift(up[-1][:cut], axis, -1), shift(down[-1][cut:], axis, 1)], axis=0
        )
        pieces = pieces + [far]
    pieces = pieces + down[1:][::-1]
    return jnp.stack(pieces, axis=0)


def direct_gather(x, axis):
    n = lax.axis_size(axis)
    return jnp.stack([x] + [shift(x, axis, -o) for o in range(1, n)], axis=0)


def local(amplitudes, pair_interaction, ph_interaction, pp_size, ph_owner):
    row_count, chan_count, hole_width = amplitudes.shape
    row_tiles, _, col_tiles = ph_owner.shape
    tile_rows = row_count // row_tiles
    tile_cols = hole_width // col_tiles
    per_dev = ph_interaction.shape[0]
    ny, nz, nc = lax.axis_size("cy"), lax.axis_size("cz"), lax.axis_size("core")
    own = lax.all_gather(ph_interaction, ("cz", "cy"), axis=0, tiled=False)
    own = own.reshape((-1,) + ph_interaction.shape[1:])
    offset = lax.axis_index("ctr") * row_count
    positions = offset + jnp.arange(row_count, dtype=jnp.int32)
    live_mask = positions[:, None] < (pp_size * tile_rows)[None, :]
    masked = jnp.where(live_mask[:, :, None], amplitudes, jnp.zeros_like(amplitudes))
    lowered = masked.astype(jnp.bfloat16)
    my_core = lax.axis_index("core")

    def place(owner):
        dev = owner // per_dev
        here = ((dev // nc % nz) * ny + dev // (nz * nc)) * per_dev + owner % per_dev
        return here, dev % nc

    slot, owner_core = place(ph_owner)
    sib_slot, _ = place(shift(ph_owner, "core", 1))
    blocks = masked.reshape(row_tiles, tile_rows, chan_count, col_tiles, tile_cols)
    slot, sib_slot, blocks, lowered = lax.optimization_barrier((slot, sib_slot, blocks, lowered))
    ladder = lax.psum_scatter(
        jnp.einsum("crk,kch->rch", pair_interaction, lowered, preferred_element_type=jnp.float32),
        "ctr",
        scatter_dimension=0,
        tiled=True,
    )
    from_sibling = shift(own[sib_slot], "core", 1)
    chosen = jnp.where((owner_core == my_core)[..., None, None], own[slot], from_sibling)
    cycle = jnp.einsum(
        "rschk,rchkl->rschl", blocks, chosen, precision=lax.Precision.HIGHEST
    ).reshape(row_count, chan_count, hole_width)
    return jnp.where(live_mask[:, :, None], ladder, jnp.zeros_like(ladder)) + cycle


def solution(mesh):
    chan_size, ctr_size = mesh.devices.shape
    cores = 2
    cz = 8
    fine = Mesh(
        mesh.devices.reshape(chan_size // (cz * cores), cz, cores, ctr_size),
        CHAN + ("ctr",),
    )
    in_specs = (
        P("ctr", CHAN, None),
        P(CHAN, None, "ctr"),
        P(CHAN, None, None),
        P(CHAN),
        P("ctr", CHAN, None),
    )
    out_specs = P("ctr", CHAN, None)
    return jax.shard_map(local, mesh=fine, in_specs=in_specs, out_specs=out_specs, check_vma=False)
```

```python
import jax
import jax.numpy as jnp
from jax import lax
from jax.sharding import Mesh
from jax.sharding import PartitionSpec as P

CHAN = ("cy", "cz", "core")


def shift(x, axis, step):
    n = lax.axis_size(axis)
    return lax.ppermute(x, axis, [(k, (k + step) % n) for k in range(n)])


def ring_gather(x, axis):
    n = lax.axis_size(axis)
    up = [x]
    down = [x]
    for _ in range((n - 1) // 2):
        up.append(shift(up[-1], axis, -1))
        down.append(shift(down[-1], axis, 1))
    pieces = up
    if n % 2 == 0:
        cut = x.shape[0] // 2
        far = jnp.concatenate(
            [shift(up[-1][:cut], axis, -1), shift(down[-1][cut:], axis, 1)], axis=0
        )
        pieces = pieces + [far]
    pieces = pieces + down[1:][::-1]
    return jnp.stack(pieces, axis=0)


def direct_gather(x, axis):
    n = lax.axis_size(axis)
    return jnp.stack([x] + [shift(x, axis, -o) for o in range(1, n)], axis=0)


def local(amplitudes, pair_interaction, ph_interaction, pp_size, ph_owner):
    row_count, chan_count, hole_width = amplitudes.shape
    row_tiles, _, col_tiles = ph_owner.shape
    tile_rows = row_count // row_tiles
    tile_cols = hole_width // col_tiles
    per_dev = ph_interaction.shape[0]
    ny, nz, nc = lax.axis_size("cy"), lax.axis_size("cz"), lax.axis_size("core")
    by_y = lax.all_gather(ph_interaction, "cy", axis=0, tiled=False)
    own = lax.all_gather(by_y, "cz", axis=0, tiled=False)
    own = own.reshape((-1,) + ph_interaction.shape[1:])
    offset = lax.axis_index("ctr") * row_count
    positions = offset + jnp.arange(row_count, dtype=jnp.int32)
    live_mask = positions[:, None] < (pp_size * tile_rows)[None, :]
    masked = jnp.where(live_mask[:, :, None], amplitudes, jnp.zeros_like(amplitudes))
    lowered = masked.astype(jnp.bfloat16)
    my_core = lax.axis_index("core")

    def place(owner):
        dev = owner // per_dev
        here = ((dev // nc % nz) * ny + dev // (nz * nc)) * per_dev + owner % per_dev
        return here, dev % nc

    slot, owner_core = place(ph_owner)
    sib_slot, _ = place(shift(ph_owner, "core", 1))
    blocks = masked.reshape(row_tiles, tile_rows, chan_count, col_tiles, tile_cols)
    slot, sib_slot, lowered = lax.optimization_barrier((slot, sib_slot, lowered))
    ladder = lax.psum_scatter(
        jnp.einsum("crk,kch->rch", pair_interaction, lowered, preferred_element_type=jnp.float32),
        "ctr",
        scatter_dimension=0,
        tiled=True,
    )
    from_sibling = shift(own[sib_slot], "core", 1)
    chosen = jnp.where((owner_core == my_core)[..., None, None], own[slot], from_sibling)
    cycle = jnp.einsum(
        "rschk,rchkl->rschl", blocks, chosen, precision=lax.Precision.HIGHEST
    ).reshape(row_count, chan_count, hole_width)
    return jnp.where(live_mask[:, :, None], ladder, jnp.zeros_like(ladder)) + cycle


def solution(mesh):
    chan_size, ctr_size = mesh.devices.shape
    cores = 2
    cz = 8
    fine = Mesh(
        mesh.devices.reshape(chan_size // (cz * cores), cz, cores, ctr_size),
        CHAN + ("ctr",),
    )
    in_specs = (
        P("ctr", CHAN, None),
        P(CHAN, None, "ctr"),
        P(CHAN, None, None),
        P(CHAN),
        P("ctr", CHAN, None),
    )
    out_specs = P("ctr", CHAN, None)
    return jax.shard_map(local, mesh=fine, in_specs=in_specs, out_specs=out_specs, check_vma=False)
```

```python
import jax
import jax.numpy as jnp
from jax import lax
from jax.sharding import Mesh
from jax.sharding import PartitionSpec as P

CHAN = ("cy", "cz", "core")


def shift(x, axis, step):
    n = lax.axis_size(axis)
    return lax.ppermute(x, axis, [(k, (k + step) % n) for k in range(n)])


def ring_gather(x, axis):
    n = lax.axis_size(axis)
    up = [x]
    down = [x]
    for _ in range((n - 1) // 2):
        up.append(shift(up[-1], axis, -1))
        down.append(shift(down[-1], axis, 1))
    pieces = up
    if n % 2 == 0:
        cut = x.shape[0] // 2
        far = jnp.concatenate(
            [shift(up[-1][:cut], axis, -1), shift(down[-1][cut:], axis, 1)], axis=0
        )
        pieces = pieces + [far]
    pieces = pieces + down[1:][::-1]
    return jnp.stack(pieces, axis=0)


def direct_gather(x, axis):
    n = lax.axis_size(axis)
    return jnp.stack([x] + [shift(x, axis, -o) for o in range(1, n)], axis=0)


def local(amplitudes, pair_interaction, ph_interaction, pp_size, ph_owner):
    row_count, chan_count, hole_width = amplitudes.shape
    row_tiles, _, col_tiles = ph_owner.shape
    tile_rows = row_count // row_tiles
    tile_cols = hole_width // col_tiles
    per_dev = ph_interaction.shape[0]
    ny, nz, nc = lax.axis_size("cy"), lax.axis_size("cz"), lax.axis_size("core")
    by_y = lax.all_gather(ph_interaction, "cy", axis=0, tiled=False)
    own = lax.all_gather(by_y, "cz", axis=0, tiled=False)
    own = own.reshape((-1,) + ph_interaction.shape[1:])
    offset = lax.axis_index("ctr") * row_count
    positions = offset + jnp.arange(row_count, dtype=jnp.int32)
    live_mask = positions[:, None] < (pp_size * tile_rows)[None, :]
    masked = jnp.where(live_mask[:, :, None], amplitudes, jnp.zeros_like(amplitudes))
    lowered = masked.astype(jnp.bfloat16)
    my_core = lax.axis_index("core")

    def place(owner):
        dev = owner // per_dev
        here = ((dev // nc % nz) * ny + dev // (nz * nc)) * per_dev + owner % per_dev
        return here, dev % nc

    slot, owner_core = place(ph_owner)
    sib_slot, _ = place(shift(ph_owner, "core", 1))
    blocks = masked.reshape(row_tiles, tile_rows, chan_count, col_tiles, tile_cols)
    slot, sib_slot, lowered = lax.optimization_barrier((slot, sib_slot, lowered))
    ladder = lax.psum_scatter(
        jnp.einsum("crk,kch->rch", pair_interaction, lowered, preferred_element_type=jnp.float32),
        "ctr",
        scatter_dimension=0,
        tiled=True,
    )
    from_sibling = shift(own[sib_slot], "core", 1)
    chosen = jnp.where((owner_core == my_core)[..., None, None], own[slot], from_sibling)
    cycle = jnp.einsum(
        "rschk,rchkl->rschl", blocks, chosen, precision=lax.Precision.HIGH
    ).reshape(row_count, chan_count, hole_width)
    return jnp.where(live_mask[:, :, None], ladder, jnp.zeros_like(ladder)) + cycle


def solution(mesh):
    chan_size, ctr_size = mesh.devices.shape
    cores = 2
    cz = 8
    fine = Mesh(
        mesh.devices.reshape(chan_size // (cz * cores), cz, cores, ctr_size),
        CHAN + ("ctr",),
    )
    in_specs = (
        P("ctr", CHAN, None),
        P(CHAN, None, "ctr"),
        P(CHAN, None, None),
        P(CHAN),
        P("ctr", CHAN, None),
    )
    out_specs = P("ctr", CHAN, None)
    return jax.shard_map(local, mesh=fine, in_specs=in_specs, out_specs=out_specs, check_vma=False)
```

```python
import jax
import jax.numpy as jnp
from jax import lax
from jax.sharding import Mesh
from jax.sharding import PartitionSpec as P

CHAN = ("cy", "czh", "czl", "core")


def shift(x, axis, step):
    n = lax.axis_size(axis)
    return lax.ppermute(x, axis, [(k, (k + step) % n) for k in range(n)])


def ring_gather(x, axis):
    n = lax.axis_size(axis)
    up = [x]
    down = [x]
    for _ in range((n - 1) // 2):
        up.append(shift(up[-1], axis, -1))
        down.append(shift(down[-1], axis, 1))
    pieces = up
    if n % 2 == 0:
        cut = x.shape[0] // 2
        far = jnp.concatenate(
            [shift(up[-1][:cut], axis, -1), shift(down[-1][cut:], axis, 1)], axis=0
        )
        pieces = pieces + [far]
    pieces = pieces + down[1:][::-1]
    return jnp.stack(pieces, axis=0)


def direct_gather(x, axis):
    n = lax.axis_size(axis)
    return jnp.stack([x] + [shift(x, axis, -o) for o in range(1, n)], axis=0)


def local(amplitudes, pair_interaction, ph_interaction, pp_size, ph_owner):
    row_count, chan_count, hole_width = amplitudes.shape
    row_tiles, _, col_tiles = ph_owner.shape
    tile_rows = row_count // row_tiles
    tile_cols = hole_width // col_tiles
    per_dev = ph_interaction.shape[0]
    ny, nc = lax.axis_size("cy"), lax.axis_size("core")
    nz = lax.axis_size("czh") * lax.axis_size("czl")
    by_y = lax.all_gather(ph_interaction, "cy", axis=0, tiled=False)
    near = lax.all_gather(by_y, "czl", axis=0, tiled=False)
    own = lax.all_gather(near, "czh", axis=0, tiled=False)
    own = own.reshape((-1,) + ph_interaction.shape[1:])
    offset = lax.axis_index("ctr") * row_count
    positions = offset + jnp.arange(row_count, dtype=jnp.int32)
    live_mask = positions[:, None] < (pp_size * tile_rows)[None, :]
    masked = jnp.where(live_mask[:, :, None], amplitudes, jnp.zeros_like(amplitudes))
    lowered = masked.astype(jnp.bfloat16)
    my_core = lax.axis_index("core")

    def place(owner):
        dev = owner // per_dev
        here = ((dev // nc % nz) * ny + dev // (nz * nc)) * per_dev + owner % per_dev
        return here, dev % nc

    slot, owner_core = place(ph_owner)
    sib_slot, _ = place(shift(ph_owner, "core", 1))
    blocks = masked.reshape(row_tiles, tile_rows, chan_count, col_tiles, tile_cols)
    slot, sib_slot, lowered = lax.optimization_barrier((slot, sib_slot, lowered))
    ladder = lax.psum_scatter(
        jnp.einsum("crk,kch->rch", pair_interaction, lowered, preferred_element_type=jnp.float32),
        "ctr",
        scatter_dimension=0,
        tiled=True,
    )
    from_sibling = shift(own[sib_slot], "core", 1)
    chosen = jnp.where((owner_core == my_core)[..., None, None], own[slot], from_sibling)
    cycle = jnp.einsum(
        "rschk,rchkl->rschl", blocks, chosen, precision=lax.Precision.HIGH
    ).reshape(row_count, chan_count, hole_width)
    return jnp.where(live_mask[:, :, None], ladder, jnp.zeros_like(ladder)) + cycle


def solution(mesh):
    chan_size, ctr_size = mesh.devices.shape
    cores = 2
    cz = 8
    fine = Mesh(
        mesh.devices.reshape(chan_size // (cz * cores), 2, cz // 2, cores, ctr_size),
        CHAN + ("ctr",),
    )
    in_specs = (
        P("ctr", CHAN, None),
        P(CHAN, None, "ctr"),
        P(CHAN, None, None),
        P(CHAN),
        P("ctr", CHAN, None),
    )
    out_specs = P("ctr", CHAN, None)
    return jax.shard_map(local, mesh=fine, in_specs=in_specs, out_specs=out_specs, check_vma=False)
```

```python
import jax
import jax.numpy as jnp
from jax import lax
from jax.sharding import Mesh
from jax.sharding import PartitionSpec as P

CHAN = ("cy", "cz", "core")


def shift(x, axis, step):
    n = lax.axis_size(axis)
    return lax.ppermute(x, axis, [(k, (k + step) % n) for k in range(n)])


def ring_gather(x, axis):
    n = lax.axis_size(axis)
    up = [x]
    down = [x]
    for _ in range((n - 1) // 2):
        up.append(shift(up[-1], axis, -1))
        down.append(shift(down[-1], axis, 1))
    pieces = up
    if n % 2 == 0:
        cut = x.shape[0] // 2
        far = jnp.concatenate(
            [shift(up[-1][:cut], axis, -1), shift(down[-1][cut:], axis, 1)], axis=0
        )
        pieces = pieces + [far]
    pieces = pieces + down[1:][::-1]
    return jnp.stack(pieces, axis=0)


def direct_gather(x, axis):
    n = lax.axis_size(axis)
    return jnp.stack([x] + [shift(x, axis, -o) for o in range(1, n)], axis=0)


def local(amplitudes, pair_interaction, ph_interaction, pp_size, ph_owner):
    row_count, chan_count, hole_width = amplitudes.shape
    row_tiles, _, col_tiles = ph_owner.shape
    tile_rows = row_count // row_tiles
    tile_cols = hole_width // col_tiles
    per_dev = ph_interaction.shape[0]
    ny, nz, nc = lax.axis_size("cy"), lax.axis_size("cz"), lax.axis_size("core")
    spread = jnp.zeros((ny,) + ph_interaction.shape, ph_interaction.dtype)
    by_y = lax.psum(spread.at[lax.axis_index("cy")].set(ph_interaction), "cy")
    own = lax.all_gather(by_y, "cz", axis=0, tiled=False)
    own = own.reshape((-1,) + ph_interaction.shape[1:])
    offset = lax.axis_index("ctr") * row_count
    positions = offset + jnp.arange(row_count, dtype=jnp.int32)
    live_mask = positions[:, None] < (pp_size * tile_rows)[None, :]
    masked = jnp.where(live_mask[:, :, None], amplitudes, jnp.zeros_like(amplitudes))
    lowered = masked.astype(jnp.bfloat16)
    my_core = lax.axis_index("core")

    def place(owner):
        dev = owner // per_dev
        here = ((dev // nc % nz) * ny + dev // (nz * nc)) * per_dev + owner % per_dev
        return here, dev % nc

    slot, owner_core = place(ph_owner)
    sib_slot, _ = place(shift(ph_owner, "core", 1))
    blocks = masked.reshape(row_tiles, tile_rows, chan_count, col_tiles, tile_cols)
    slot, sib_slot, lowered = lax.optimization_barrier((slot, sib_slot, lowered))
    ladder = lax.psum_scatter(
        jnp.einsum("crk,kch->rch", pair_interaction, lowered, preferred_element_type=jnp.float32),
        "ctr",
        scatter_dimension=0,
        tiled=True,
    )
    from_sibling = shift(own[sib_slot], "core", 1)
    chosen = jnp.where((owner_core == my_core)[..., None, None], own[slot], from_sibling)
    cycle = jnp.einsum(
        "rschk,rchkl->rschl", blocks, chosen, precision=lax.Precision.HIGH
    ).reshape(row_count, chan_count, hole_width)
    return jnp.where(live_mask[:, :, None], ladder, jnp.zeros_like(ladder)) + cycle


def solution(mesh):
    chan_size, ctr_size = mesh.devices.shape
    cores = 2
    cz = 8
    fine = Mesh(
        mesh.devices.reshape(chan_size // (cz * cores), cz, cores, ctr_size),
        CHAN + ("ctr",),
    )
    in_specs = (
        P("ctr", CHAN, None),
        P(CHAN, None, "ctr"),
        P(CHAN, None, None),
        P(CHAN),
        P("ctr", CHAN, None),
    )
    out_specs = P("ctr", CHAN, None)
    return jax.shard_map(local, mesh=fine, in_specs=in_specs, out_specs=out_specs, check_vma=False)
```

```python
import jax
import jax.numpy as jnp
from jax import lax
from jax.sharding import Mesh
from jax.sharding import PartitionSpec as P

CHAN = ("cy", "cz", "core")


def shift(x, axis, step):
    n = lax.axis_size(axis)
    return lax.ppermute(x, axis, [(k, (k + step) % n) for k in range(n)])


def ring_gather(x, axis):
    n = lax.axis_size(axis)
    up = [x]
    down = [x]
    for _ in range((n - 1) // 2):
        up.append(shift(up[-1], axis, -1))
        down.append(shift(down[-1], axis, 1))
    pieces = up
    if n % 2 == 0:
        cut = x.shape[0] // 2
        far = jnp.concatenate(
            [shift(up[-1][:cut], axis, -1), shift(down[-1][cut:], axis, 1)], axis=0
        )
        pieces = pieces + [far]
    pieces = pieces + down[1:][::-1]
    return jnp.stack(pieces, axis=0)


def direct_gather(x, axis):
    n = lax.axis_size(axis)
    return jnp.stack([x] + [shift(x, axis, -o) for o in range(1, n)], axis=0)


def local(amplitudes, pair_interaction, ph_interaction, pp_size, ph_owner):
    row_count, chan_count, hole_width = amplitudes.shape
    row_tiles, _, col_tiles = ph_owner.shape
    tile_rows = row_count // row_tiles
    tile_cols = hole_width // col_tiles
    per_dev = ph_interaction.shape[0]
    ny, nz, nc = lax.axis_size("cy"), lax.axis_size("cz"), lax.axis_size("core")
    by_y = lax.all_gather(ph_interaction, "cy", axis=0, tiled=False)
    own = lax.all_gather(by_y, "cz", axis=0, tiled=False)
    own = own.reshape((-1,) + ph_interaction.shape[1:])
    offset = lax.axis_index("ctr") * row_count
    positions = offset + jnp.arange(row_count, dtype=jnp.int32)
    live_mask = positions[:, None] < (pp_size * tile_rows)[None, :]
    masked = jnp.where(live_mask[:, :, None], amplitudes, jnp.zeros_like(amplitudes))
    lowered = masked.astype(jnp.bfloat16)
    my_core = lax.axis_index("core")

    def place(owner):
        dev = owner // per_dev
        here = ((dev // nc % nz) * ny + dev // (nz * nc)) * per_dev + owner % per_dev
        return here, dev % nc

    slot, owner_core = place(ph_owner)
    sib_slot, _ = place(shift(ph_owner, "core", 1))
    blocks = masked.reshape(row_tiles, tile_rows, chan_count, col_tiles, tile_cols)
    slot, sib_slot, lowered = lax.optimization_barrier((slot, sib_slot, lowered))
    half = hole_width // 2
    parts = [
        jnp.einsum(
            "crk,kch->rch", pair_interaction, lowered[:, :, s : s + half],
            preferred_element_type=jnp.float32,
        )
        for s in (0, half)
    ]
    parts[0], masked_late = lax.optimization_barrier((parts[0], masked))
    blocks = masked_late.reshape(row_tiles, tile_rows, chan_count, col_tiles, tile_cols)
    ladder = jnp.concatenate(
        [lax.psum_scatter(p, "ctr", scatter_dimension=0, tiled=True) for p in parts], axis=2
    )
    from_sibling = shift(own[sib_slot], "core", 1)
    chosen = jnp.where((owner_core == my_core)[..., None, None], own[slot], from_sibling)
    cycle = jnp.einsum(
        "rschk,rchkl->rschl", blocks, chosen, precision=lax.Precision.HIGH
    ).reshape(row_count, chan_count, hole_width)
    return jnp.where(live_mask[:, :, None], ladder, jnp.zeros_like(ladder)) + cycle


def solution(mesh):
    chan_size, ctr_size = mesh.devices.shape
    cores = 2
    cz = 8
    fine = Mesh(
        mesh.devices.reshape(chan_size // (cz * cores), cz, cores, ctr_size),
        CHAN + ("ctr",),
    )
    in_specs = (
        P("ctr", CHAN, None),
        P(CHAN, None, "ctr"),
        P(CHAN, None, None),
        P(CHAN),
        P("ctr", CHAN, None),
    )
    out_specs = P("ctr", CHAN, None)
    return jax.shard_map(local, mesh=fine, in_specs=in_specs, out_specs=out_specs, check_vma=False)
```

```python
import jax
import jax.numpy as jnp
from jax import lax
from jax.experimental import pallas as pl
from jax.sharding import Mesh
from jax.sharding import PartitionSpec as P

CHAN = ("cy", "cz", "core")


def shift(x, axis, step):
    n = lax.axis_size(axis)
    return lax.ppermute(x, axis, [(k, (k + step) % n) for k in range(n)])


def ring_gather(x, axis):
    n = lax.axis_size(axis)
    up = [x]
    down = [x]
    for _ in range((n - 1) // 2):
        up.append(shift(up[-1], axis, -1))
        down.append(shift(down[-1], axis, 1))
    pieces = up
    if n % 2 == 0:
        cut = x.shape[0] // 2
        far = jnp.concatenate(
            [shift(up[-1][:cut], axis, -1), shift(down[-1][cut:], axis, 1)], axis=0
        )
        pieces = pieces + [far]
    pieces = pieces + down[1:][::-1]
    return jnp.stack(pieces, axis=0)


def direct_gather(x, axis):
    n = lax.axis_size(axis)
    return jnp.stack([x] + [shift(x, axis, -o) for o in range(1, n)], axis=0)


def ladder_kernel(lt_ref, p_ref, o_ref):
    o_ref[...] = lax.dot_general(
        lt_ref[...], p_ref[...], (((1,), (1,)), ((), ())), preferred_element_type=jnp.float32
    )


def ladder_matmul_t(lowered_t, weights, block=512):
    width, depth = lowered_t.shape
    rows = weights.shape[0]
    return pl.pallas_call(
        ladder_kernel,
        grid=(rows // block,),
        in_specs=[
            pl.BlockSpec((width, depth), lambda i: (0, 0)),
            pl.BlockSpec((block, depth), lambda i: (i, 0)),
        ],
        out_specs=pl.BlockSpec((width, block), lambda i: (0, i)),
        out_shape=jax.ShapeDtypeStruct((width, rows), jnp.float32),
        cost_estimate=pl.CostEstimate(
            flops=2 * rows * depth * width,
            bytes_accessed=2 * rows * depth + 2 * depth * width + 4 * rows * width,
            transcendentals=0,
        ),
    )(lowered_t, weights)


def local(amplitudes, pair_interaction, ph_interaction, pp_size, ph_owner):
    row_count, chan_count, hole_width = amplitudes.shape
    row_tiles, _, col_tiles = ph_owner.shape
    tile_rows = row_count // row_tiles
    tile_cols = hole_width // col_tiles
    per_dev = ph_interaction.shape[0]
    ny, nz, nc = lax.axis_size("cy"), lax.axis_size("cz"), lax.axis_size("core")
    by_y = lax.all_gather(ph_interaction, "cy", axis=0, tiled=False)
    own = lax.all_gather(by_y, "cz", axis=0, tiled=False)
    own = own.reshape((-1,) + ph_interaction.shape[1:])
    offset = lax.axis_index("ctr") * row_count
    positions = offset + jnp.arange(row_count, dtype=jnp.int32)
    live_mask = positions[:, None] < (pp_size * tile_rows)[None, :]
    masked = jnp.where(live_mask[:, :, None], amplitudes, jnp.zeros_like(amplitudes))
    lowered = masked.astype(jnp.bfloat16)
    my_core = lax.axis_index("core")

    def place(owner):
        dev = owner // per_dev
        here = ((dev // nc % nz) * ny + dev // (nz * nc)) * per_dev + owner % per_dev
        return here, dev % nc

    slot, owner_core = place(ph_owner)
    sib_slot, _ = place(shift(ph_owner, "core", 1))
    blocks = masked.reshape(row_tiles, tile_rows, chan_count, col_tiles, tile_cols)
    slot, sib_slot, lowered = lax.optimization_barrier((slot, sib_slot, lowered))
    ladder = lax.psum_scatter(
        jnp.transpose(
            ladder_matmul_t(lowered[:, 0, :].T, pair_interaction[0])
        )[:, None, :],
        "ctr",
        scatter_dimension=0,
        tiled=True,
    )
    from_sibling = shift(own[sib_slot], "core", 1)
    chosen = jnp.where((owner_core == my_core)[..., None, None], own[slot], from_sibling)
    cycle = jnp.einsum(
        "rschk,rchkl->rschl", blocks, chosen, precision=lax.Precision.HIGH
    ).reshape(row_count, chan_count, hole_width)
    return jnp.where(live_mask[:, :, None], ladder, jnp.zeros_like(ladder)) + cycle


def solution(mesh):
    chan_size, ctr_size = mesh.devices.shape
    cores = 2
    cz = 8
    fine = Mesh(
        mesh.devices.reshape(chan_size // (cz * cores), cz, cores, ctr_size),
        CHAN + ("ctr",),
    )
    in_specs = (
        P("ctr", CHAN, None),
        P(CHAN, None, "ctr"),
        P(CHAN, None, None),
        P(CHAN),
        P("ctr", CHAN, None),
    )
    out_specs = P("ctr", CHAN, None)
    return jax.shard_map(local, mesh=fine, in_specs=in_specs, out_specs=out_specs, check_vma=False)
```

```python
import jax
import jax.numpy as jnp
from jax import lax
from jax.experimental import pallas as pl
from jax.sharding import Mesh
from jax.sharding import PartitionSpec as P

CHAN = ("cy", "cz", "core")


def shift(x, axis, step):
    n = lax.axis_size(axis)
    return lax.ppermute(x, axis, [(k, (k + step) % n) for k in range(n)])


def ring_gather(x, axis):
    n = lax.axis_size(axis)
    up = [x]
    down = [x]
    for _ in range((n - 1) // 2):
        up.append(shift(up[-1], axis, -1))
        down.append(shift(down[-1], axis, 1))
    pieces = up
    if n % 2 == 0:
        cut = x.shape[0] // 2
        far = jnp.concatenate(
            [shift(up[-1][:cut], axis, -1), shift(down[-1][cut:], axis, 1)], axis=0
        )
        pieces = pieces + [far]
    pieces = pieces + down[1:][::-1]
    return jnp.stack(pieces, axis=0)


def direct_gather(x, axis):
    n = lax.axis_size(axis)
    return jnp.stack([x] + [shift(x, axis, -o) for o in range(1, n)], axis=0)


def ladder_kernel(lt_ref, p_ref, o_ref):
    o_ref[...] = lax.dot_general(
        lt_ref[...], p_ref[...], (((1,), (1,)), ((), ())), preferred_element_type=jnp.float32
    )


def ladder_matmul_t(lowered_t, weights, block=512):
    width, depth = lowered_t.shape
    rows = weights.shape[0]
    return pl.pallas_call(
        ladder_kernel,
        grid=(rows // block,),
        in_specs=[
            pl.BlockSpec((width, depth), lambda i: (0, 0)),
            pl.BlockSpec((block, depth), lambda i: (i, 0)),
        ],
        out_specs=pl.BlockSpec((width, block), lambda i: (0, i)),
        out_shape=jax.ShapeDtypeStruct((width, rows), jnp.float32),
        cost_estimate=pl.CostEstimate(
            flops=2 * rows * depth * width,
            bytes_accessed=2 * rows * depth + 2 * depth * width + 4 * rows * width,
            transcendentals=0,
        ),
    )(lowered_t, weights)


def local(amplitudes, pair_interaction, ph_interaction, pp_size, ph_owner):
    row_count, chan_count, hole_width = amplitudes.shape
    row_tiles, _, col_tiles = ph_owner.shape
    tile_rows = row_count // row_tiles
    tile_cols = hole_width // col_tiles
    per_dev = ph_interaction.shape[0]
    ny, nz, nc = lax.axis_size("cy"), lax.axis_size("cz"), lax.axis_size("core")
    by_y = lax.all_gather(ph_interaction, "cy", axis=0, tiled=False)
    own = lax.all_gather(by_y, "cz", axis=0, tiled=False)
    own = own.reshape((-1,) + ph_interaction.shape[1:])
    offset = lax.axis_index("ctr") * row_count
    positions = offset + jnp.arange(row_count, dtype=jnp.int32)
    live_mask = positions[:, None] < (pp_size * tile_rows)[None, :]
    masked = jnp.where(live_mask[:, :, None], amplitudes, jnp.zeros_like(amplitudes))
    lowered = masked.astype(jnp.bfloat16)
    my_core = lax.axis_index("core")

    def place(owner):
        dev = owner // per_dev
        here = ((dev // nc % nz) * ny + dev // (nz * nc)) * per_dev + owner % per_dev
        return here, dev % nc

    slot, owner_core = place(ph_owner)
    sib_slot, _ = place(shift(ph_owner, "core", 1))
    slot, sib_slot, lowered = lax.optimization_barrier((slot, sib_slot, lowered))
    partial = ladder_matmul_t(lowered[:, 0, :].T, pair_interaction[0])
    partial, masked_late = lax.optimization_barrier((partial, masked))
    blocks = masked_late.reshape(row_tiles, tile_rows, chan_count, col_tiles, tile_cols)
    blocks, own = lax.optimization_barrier((blocks, own))
    ladder = lax.psum_scatter(
        jnp.transpose(partial)[:, None, :],
        "ctr",
        scatter_dimension=0,
        tiled=True,
    )
    from_sibling = shift(own[sib_slot], "core", 1)
    chosen = jnp.where((owner_core == my_core)[..., None, None], own[slot], from_sibling)
    cycle = jnp.einsum(
        "rschk,rchkl->rschl", blocks, chosen, precision=lax.Precision.HIGH
    ).reshape(row_count, chan_count, hole_width)
    return jnp.where(live_mask[:, :, None], ladder, jnp.zeros_like(ladder)) + cycle


def solution(mesh):
    chan_size, ctr_size = mesh.devices.shape
    cores = 2
    cz = 8
    fine = Mesh(
        mesh.devices.reshape(chan_size // (cz * cores), cz, cores, ctr_size),
        CHAN + ("ctr",),
    )
    in_specs = (
        P("ctr", CHAN, None),
        P(CHAN, None, "ctr"),
        P(CHAN, None, None),
        P(CHAN),
        P("ctr", CHAN, None),
    )
    out_specs = P("ctr", CHAN, None)
    return jax.shard_map(local, mesh=fine, in_specs=in_specs, out_specs=out_specs, check_vma=False)
```

```python
import jax
import jax.numpy as jnp
from jax import lax
from jax.experimental import pallas as pl
from jax.sharding import Mesh
from jax.sharding import PartitionSpec as P

CHAN = ("cy", "cz", "core")


def shift(x, axis, step):
    n = lax.axis_size(axis)
    return lax.ppermute(x, axis, [(k, (k + step) % n) for k in range(n)])


def ring_gather(x, axis):
    n = lax.axis_size(axis)
    up = [x]
    down = [x]
    for _ in range((n - 1) // 2):
        up.append(shift(up[-1], axis, -1))
        down.append(shift(down[-1], axis, 1))
    pieces = up
    if n % 2 == 0:
        cut = x.shape[0] // 2
        far = jnp.concatenate(
            [shift(up[-1][:cut], axis, -1), shift(down[-1][cut:], axis, 1)], axis=0
        )
        pieces = pieces + [far]
    pieces = pieces + down[1:][::-1]
    return jnp.stack(pieces, axis=0)


def direct_gather(x, axis):
    n = lax.axis_size(axis)
    return jnp.stack([x] + [shift(x, axis, -o) for o in range(1, n)], axis=0)


def ladder_kernel(lt_ref, p_ref, o_ref):
    o_ref[...] = lax.dot_general(
        lt_ref[...], p_ref[...], (((1,), (1,)), ((), ())), preferred_element_type=jnp.float32
    )


def ladder_matmul_t(lowered_t, weights, block=512):
    width, depth = lowered_t.shape
    rows = weights.shape[0]
    return pl.pallas_call(
        ladder_kernel,
        grid=(rows // block,),
        in_specs=[
            pl.BlockSpec((width, depth), lambda i: (0, 0)),
            pl.BlockSpec((block, depth), lambda i: (i, 0)),
        ],
        out_specs=pl.BlockSpec((width, block), lambda i: (0, i)),
        out_shape=jax.ShapeDtypeStruct((width, rows), jnp.float32),
        cost_estimate=pl.CostEstimate(
            flops=2 * rows * depth * width,
            bytes_accessed=2 * rows * depth + 2 * depth * width + 4 * rows * width,
            transcendentals=0,
        ),
    )(lowered_t, weights)


def local(amplitudes, pair_interaction, ph_interaction, pp_size, ph_owner):
    row_count, chan_count, hole_width = amplitudes.shape
    row_tiles, _, col_tiles = ph_owner.shape
    tile_rows = row_count // row_tiles
    tile_cols = hole_width // col_tiles
    per_dev = ph_interaction.shape[0]
    ny, nz, nc = lax.axis_size("cy"), lax.axis_size("cz"), lax.axis_size("core")
    by_y = lax.all_gather(ph_interaction, "cy", axis=0, tiled=False)
    own = lax.all_gather(by_y, "cz", axis=0, tiled=False)
    own = own.reshape((-1,) + ph_interaction.shape[1:])
    offset = lax.axis_index("ctr") * row_count
    positions = offset + jnp.arange(row_count, dtype=jnp.int32)
    live_mask = positions[:, None] < (pp_size * tile_rows)[None, :]
    masked = jnp.where(live_mask[:, :, None], amplitudes, jnp.zeros_like(amplitudes))
    lowered = masked.astype(jnp.bfloat16)
    my_core = lax.axis_index("core")

    def place(owner):
        dev = owner // per_dev
        here = ((dev // nc % nz) * ny + dev // (nz * nc)) * per_dev + owner % per_dev
        return here, dev % nc

    slot, owner_core = place(ph_owner)
    sib_slot, _ = place(shift(ph_owner, "core", 1))
    slot, sib_slot, lowered = lax.optimization_barrier((slot, sib_slot, lowered))
    partial = ladder_matmul_t(lowered[:, 0, :].T, pair_interaction[0])
    partial, masked_late = lax.optimization_barrier((partial, masked))
    blocks = masked_late.reshape(row_tiles, tile_rows, chan_count, col_tiles, tile_cols)
    blocks, own = lax.optimization_barrier((blocks, own))
    ladder = lax.psum_scatter(
        jnp.transpose(partial)[:, None, :],
        "ctr",
        scatter_dimension=0,
        tiled=True,
    )
    cut = sib_slot.shape[0] // 2
    from_sibling = jnp.concatenate(
        [shift(own[sib_slot[:cut]], "core", 1), shift(own[sib_slot[cut:]], "core", 1)], axis=0
    )
    chosen = jnp.where((owner_core == my_core)[..., None, None], own[slot], from_sibling)
    cycle = jnp.einsum(
        "rschk,rchkl->rschl", blocks, chosen, precision=lax.Precision.HIGH
    ).reshape(row_count, chan_count, hole_width)
    return jnp.where(live_mask[:, :, None], ladder, jnp.zeros_like(ladder)) + cycle


def solution(mesh):
    chan_size, ctr_size = mesh.devices.shape
    cores = 2
    cz = 8
    fine = Mesh(
        mesh.devices.reshape(chan_size // (cz * cores), cz, cores, ctr_size),
        CHAN + ("ctr",),
    )
    in_specs = (
        P("ctr", CHAN, None),
        P(CHAN, None, "ctr"),
        P(CHAN, None, None),
        P(CHAN),
        P("ctr", CHAN, None),
    )
    out_specs = P("ctr", CHAN, None)
    return jax.shard_map(local, mesh=fine, in_specs=in_specs, out_specs=out_specs, check_vma=False)
```
